512 devices in a mesh: heads: 8 (over y, core), seq: 64 (over z, x).
Axes of the slice: x: 4, y: 4, z: 16, core: 2. Of those that a mesh axis runs over, the one named last changes fastest.
Arguments:
- query_proj: bfloat16 [8192, 4096], P('seq', 'heads'), may hold values from -6 to 6
- key_proj: bfloat16 [8192, 4096], P('seq', 'heads'), may hold values from -6 to 6
- value_proj: bfloat16 [8192, 4096], P('seq', 'heads'), may hold values from -6 to 6
- gate_proj: bfloat16 [8192, 4096], P('seq', 'heads'), may hold values from -6 to 6
- write_rate: float32 [32, 8192], P('heads', 'seq'), may hold values from 0 to 1
- log_decay: float32 [32, 8192], P('heads', 'seq'), may hold values from -1 to 0
- doc_start: int32 [8192], P('seq'), may hold values from 0 to 1, as said below
- norm_gain: float32 [128], replicated, may hold values from 0.5 to 1.5
- out_weight: bfloat16 [4096, 4096], P('heads', 'seq'), may hold values from -0.09375 to 0.09375
Outputs:
- layer_out: bfloat16 [8192, 4096], P('seq', 'heads')
The draws below stay inside these ranges and needn't reach their ends.
Inputs may be any that keep to these rules, and one draw needn't show every extreme that they name: `doc_start`: exactly two entries are 1: one in the first half of the sequence (never token 0) and one in the second half.
All inputs are finite; a program needn't handle non-finite values.
Results may differ from the reference program's by a relative error of at most 0.017.
Values may be sent and summed in bfloat16 or wider, within the bound.
No kernel may reach another device: no remote copies, remote signals or barrier semaphores. Data moves between devices by JAX's collectives and lax.ppermute only.
A program may use at most 128 MiB of HBM per device.

```python
import jax
import jax.numpy as jnp
from jax import lax

D = 4096
H = 32
DK = 128
DV = 128
STRETCH = 64
TOKENS = 8192
N_HEADS = 8


def draw_log_decay(key, part):
    order = jax.random.permutation(jax.random.fold_in(key, 11), H)
    slow = order >= H // 2
    slow_rate = -jax.random.uniform(jax.random.fold_in(key, 1), (H, TOKENS), jnp.float32, 0.25, 1.0) * 1.15 / TOKENS
    fast_rate = -jnp.exp(jax.random.uniform(jax.random.fold_in(key, 2), (H, TOKENS), jnp.float32, -0.69, 0.69)) * 0.0576
    start_index_shift = jnp.where(slow[:, None], slow_rate, fast_rate)
    cache_place_indices = jax.random.randint(jax.random.fold_in(key, 3), (H, 2), 0, TOKENS)
    element_ordinals = jnp.arange(TOKENS)
    document_span_piece = jnp.any(cache_place_indices[:, :, None] == element_ordinals[None, None, :], axis=1)
    learning_loss_target = jnp.log(jax.random.uniform(jax.random.fold_in(key, 4), (H, TOKENS), jnp.float32, 0.5, 0.8))
    return jnp.where(document_span_piece, start_index_shift + learning_loss_target, start_index_shift).astype(jnp.float32)


def draw_write_rate(key, part):
    order = jax.random.permutation(jax.random.fold_in(key, 11), H)
    slow = order >= H // 2
    slow_rate = jax.random.uniform(jax.random.fold_in(key, 5), (H, TOKENS), jnp.float32, 0.25, 1.0) * DK / (2.0 * TOKENS)
    fast_rate = jax.random.uniform(jax.random.fold_in(key, 6), (H, TOKENS), jnp.float32, 0.2, 0.9)
    return jnp.where(slow[:, None], slow_rate, fast_rate).astype(jnp.float32)


def draw_doc_start(key, part):
    first_spot = jax.random.randint(jax.random.fold_in(key, 21), (), 1, TOKENS // 2)
    second_spot = jax.random.randint(jax.random.fold_in(key, 22), (), TOKENS // 2, TOKENS)
    element_ordinals = jnp.arange(TOKENS)
    return ((element_ordinals == first_spot) | (element_ordinals == second_spot)).astype(jnp.int32)


def steps_of(stream_key, shape, pieces, smallest, largest):
    level = 1.0
    for dim, shards_of in pieces:
        heights = jax.random.uniform(jax.random.fold_in(jax.random.fold_in(stream_key, 6), dim), (shards_of,), jnp.float32, smallest / len(pieces), largest / len(pieces))
        level = level * jnp.repeat(jnp.exp(heights), shape[dim] // shards_of).reshape((-1,) + (1,) * (len(shape) - 1 - dim))
    return level


def noise(stream_key, dims, deviation, most, split=(), held_as=jnp.bfloat16):
    result = jax.random.normal(stream_key, dims, jnp.float32) * deviation
    if len(split) > 0:
        result = steps_of(stream_key, dims, split, -0.22, 0.18) * result
    return jnp.clip(result, min=-most, max=most).astype(held_as)


def setup_inputs(seed: int = 0) -> dict:
    splits = jax.random.split(jax.random.key(seed), 10)
    return {
        "query_proj": noise(splits[0], (TOKENS, H * DK), 1.0, 6.0, ((0, 64), (1, 8))),
        "key_proj": noise(splits[1], (TOKENS, H * DK), 1.0, 6.0, ((0, 64), (1, 8))),
        "value_proj": noise(splits[2], (TOKENS, H * DV), 1.0, 6.0, ((0, 64), (1, 8))),
        "gate_proj": noise(splits[3], (TOKENS, H * DV), 1.0, 6.0, ((0, 64), (1, 8))),
        "write_rate": draw_write_rate(jax.random.fold_in(splits[9], 71), 0),
        "log_decay": draw_log_decay(jax.random.fold_in(splits[9], 71), 0),
        "doc_start": draw_doc_start(jax.random.fold_in(splits[9], 71), 0),
        "norm_gain": jnp.clip(1.0 + 0.1 * jax.random.normal(splits[7], (DV,), jnp.float32), 0.5, 1.5),
        "out_weight": noise(splits[8], (H * DV, D), (H * DV) ** -0.5, 0.09375, ((0, 8), (1, 64))),
    }


precise = lax.Precision.HIGHEST
epsilon = 1e-06

def unit_rows(block):
    return block / jnp.sqrt(lax.optimization_barrier(jnp.sum(block * block, axis=-1, keepdims=True)) + epsilon)

def triangular_inverse_below(system, right_side):
    return jax.scipy.linalg.solve_triangular(system, right_side, lower=True, unit_diagonal=True)

def stretch_terms(queries, keys_normed, values_in, rates, decays, resets):
    length = queries.shape[-2]
    cumulated = jnp.cumsum(decays, axis=-1)
    seen = jnp.cumsum(resets, axis=-1)
    row_index = lax.broadcasted_iota(jnp.int32, (length, length), 0)
    col_index = lax.broadcasted_iota(jnp.int32, (length, length), 1)
    same_span = (seen[..., :, None] == seen[..., None, :]) & (row_index >= col_index)
    log_gap = jnp.where(same_span, cumulated[..., :, None] - cumulated[..., None, :], 0.0)
    pair_decay = jnp.where(same_span, jnp.exp(log_gap), 0.0)
    head_decay = jnp.exp(cumulated) * (seen == 0).astype(jnp.float32)
    tail_decay = jnp.exp(cumulated[..., -1:] - cumulated) * (seen[..., -1:] == seen).astype(jnp.float32)
    key_gram = jnp.einsum('...cd,...md->...cm', keys_normed, keys_normed, precision=precise)
    strict_part = jnp.where(row_index > col_index, rates[..., :, None] * pair_decay * key_gram, 0.0)
    system = strict_part + jnp.eye(length, dtype=jnp.float32)
    pseudo_values = triangular_inverse_below(system, rates[..., None] * values_in)
    key_weights = triangular_inverse_below(system, (rates * head_decay)[..., None] * keys_normed)
    scores = pair_decay * jnp.einsum('...cd,...md->...cm', queries, keys_normed, precision=precise)
    query_state = head_decay[..., None] * queries - jnp.einsum('...cm,...md->...cd', scores, key_weights, precision=precise)
    local_out = jnp.einsum('...cm,...md->...cd', scores, pseudo_values, precision=precise)
    identity = jnp.eye(keys_normed.shape[-1], dtype=jnp.float32)
    transit = head_decay[..., -1][..., None, None] * identity - jnp.einsum('...cd,...ce->...de', keys_normed, tail_decay[..., None] * key_weights, precision=precise)
    written = jnp.einsum('...cd,...ce->...de', keys_normed, tail_decay[..., None] * pseudo_values, precision=precise)
    return (query_state, local_out, transit, written)

def gated_norm(core_out, gate_block, gain):
    scale = lax.rsqrt(lax.optimization_barrier(jnp.mean(core_out * core_out, axis=-1, keepdims=True)) + epsilon)
    gate_float = gate_block.astype(jnp.float32)
    return (core_out * scale * gain * jax.nn.silu(gate_float)).astype(jnp.bfloat16)

def reference(query_proj, key_proj, value_proj, gate_proj, write_rate, log_decay, doc_start, norm_gain, out_weight):
    blocks = TOKENS // STRETCH
    inputs_all = (query_proj.reshape(blocks, STRETCH, H, DK), key_proj.reshape(blocks, STRETCH, H, DK), value_proj.reshape(blocks, STRETCH, H, DV), gate_proj.reshape(blocks, STRETCH, H, DV), write_rate.reshape(H, blocks, STRETCH).transpose(1, 0, 2), log_decay.reshape(H, blocks, STRETCH).transpose(1, 0, 2), doc_start.reshape(blocks, STRETCH))

    def advance(carried_state, inputs):
        question_tile_rows, key_block, value_block, gate_block, rates, decays, resets = inputs
        queries = unit_rows(question_tile_rows.astype(jnp.float32)).transpose(1, 0, 2)
        keys_normed = unit_rows(key_block.astype(jnp.float32)).transpose(1, 0, 2)
        values_in = value_block.astype(jnp.float32).transpose(1, 0, 2)
        query_state, local_out, transit, written = stretch_terms(queries, keys_normed, values_in, rates, decays, resets[None, :])
        core_out = jnp.einsum('hcd,hde->hce', query_state, carried_state, precision=precise) + local_out
        next_state = jnp.einsum('hde,hef->hdf', transit, carried_state, precision=precise) + written
        normed = gated_norm(core_out.transpose(1, 0, 2), gate_block, norm_gain)
        return (next_state, normed.reshape(STRETCH, H * DV))
    start_state = jnp.zeros((H, DK, DV), jnp.float32)
    unused_state, normed = lax.scan(advance, start_state, inputs_all)
    normed = normed.reshape(TOKENS, H * DV)
    group_width = H * DV // N_HEADS
    summed = jnp.zeros((TOKENS, D), jnp.float32)
    for group_index in range(N_HEADS):
        low = group_index * group_width
        partial_value = jnp.dot(normed[:, low:low + group_width].astype(jnp.float32), out_weight[low:low + group_width, :].astype(jnp.float32), preferred_element_type=jnp.float32).astype(jnp.bfloat16)
        partial_value = lax.optimization_barrier(partial_value)
        summed = summed + partial_value.astype(jnp.float32)
    return summed.astype(jnp.bfloat16)
```

```python
import jax
import jax.numpy as jnp
from jax import lax
from jax.sharding import Mesh
from jax.sharding import PartitionSpec as P

STRETCH = 64
SEQ_MINOR = 4


precise = lax.Precision.HIGHEST
epsilon = 1e-06


def unit_rows(block):
    return block / jnp.sqrt(jnp.sum(block * block, axis=-1, keepdims=True) + epsilon)


def triangular_inverse_below(system, right_side):
    return jax.scipy.linalg.solve_triangular(system, right_side, lower=True, unit_diagonal=True)


def matrix_product(left_side, right_side):
    return jnp.einsum("...de,...ef->...df", left_side, right_side, precision=precise)


def stretch_terms(queries, keys_normed, values_in, rates, decays, resets):
    length = queries.shape[-2]
    value_width = values_in.shape[-1]
    cumulated = jnp.cumsum(decays, axis=-1)
    seen = jnp.cumsum(resets, axis=-1)
    row_index = lax.broadcasted_iota(jnp.int32, (length, length), 0)
    col_index = lax.broadcasted_iota(jnp.int32, (length, length), 1)
    same_span = (seen[..., :, None] == seen[..., None, :]) & (row_index >= col_index)
    log_gap = jnp.where(same_span, cumulated[..., :, None] - cumulated[..., None, :], 0.0)
    pair_decay = jnp.where(same_span, jnp.exp(log_gap), 0.0)
    head_decay = jnp.exp(cumulated) * (seen == 0).astype(jnp.float32)
    tail_decay = jnp.exp(cumulated[..., -1:] - cumulated) * (seen[..., -1:] == seen).astype(
        jnp.float32
    )
    key_gram = jnp.einsum("...cd,...md->...cm", keys_normed, keys_normed, precision=precise)
    strict_part = jnp.where(row_index > col_index, rates[..., :, None] * pair_decay * key_gram, 0.0)
    system = strict_part + jnp.eye(length, dtype=jnp.float32)
    both_sides = jnp.concatenate(
        [rates[..., None] * values_in, (rates * head_decay)[..., None] * keys_normed], axis=-1
    )
    solved = triangular_inverse_below(system, both_sides)
    pseudo_values = solved[..., :value_width]
    key_weights = solved[..., value_width:]
    scores = pair_decay * jnp.einsum("...cd,...md->...cm", queries, keys_normed, precision=precise)
    query_state = head_decay[..., None] * queries - jnp.einsum(
        "...cm,...md->...cd", scores, key_weights, precision=precise
    )
    local_out = jnp.einsum("...cm,...md->...cd", scores, pseudo_values, precision=precise)
    identity = jnp.eye(keys_normed.shape[-1], dtype=jnp.float32)
    transit = head_decay[..., -1][..., None, None] * identity - jnp.einsum(
        "...cd,...ce->...de", keys_normed, tail_decay[..., None] * key_weights, precision=precise
    )
    written = jnp.einsum(
        "...cd,...ce->...de", keys_normed, tail_decay[..., None] * pseudo_values, precision=precise
    )
    return (query_state, local_out, transit, written)


def gated_norm(core_out, gate_block, gain):
    scale = lax.rsqrt(jnp.mean(core_out * core_out, axis=-1, keepdims=True) + epsilon)
    gate_float = gate_block.astype(jnp.float32)
    return (core_out * scale * gain * jax.nn.silu(gate_float)).astype(jnp.bfloat16)


def shift_down(array, step, fill):
    head = jnp.broadcast_to(fill, (step,) + array.shape[1:]).astype(array.dtype)
    return jnp.concatenate([head, array[:-step]], axis=0)


def on_device(
    query_proj,
    key_proj,
    value_proj,
    gate_proj,
    write_rate,
    log_decay,
    doc_start,
    norm_gain,
    out_weight,
    minor,
    major,
):
    head_count = write_rate.shape[0]
    key_width = query_proj.shape[1] // head_count
    value_width = value_proj.shape[1] // head_count

    def spread(array):
        return lax.all_to_all(array, "x", 1, 0, tiled=True)

    query_here = spread(query_proj)
    key_here = spread(key_proj)
    value_here = spread(value_proj)
    gate_here = spread(gate_proj)
    rates_here = lax.all_to_all(write_rate, "x", 0, 1, tiled=True)
    decays_here = lax.all_to_all(log_decay, "x", 0, 1, tiled=True)
    resets_here = lax.all_gather(doc_start, "x", tiled=True)

    tok_rows = query_here.shape[0]
    local_heads = head_count // minor
    blocks = tok_rows // STRETCH

    def stretch_major(array, width):
        return array.reshape(blocks, STRETCH, local_heads, width).transpose(0, 2, 1, 3)

    queries = unit_rows(stretch_major(query_here, key_width).astype(jnp.float32))
    keys_normed = unit_rows(stretch_major(key_here, key_width).astype(jnp.float32))
    values_in = stretch_major(value_here, value_width).astype(jnp.float32)
    rates = rates_here.reshape(local_heads, blocks, STRETCH).transpose(1, 0, 2)
    decays = decays_here.reshape(local_heads, blocks, STRETCH).transpose(1, 0, 2)
    resets = resets_here.reshape(blocks, 1, STRETCH)
    query_state, local_out, transit, written = stretch_terms(
        queries, keys_normed, values_in, rates, decays, resets
    )
    identity = jnp.eye(key_width, dtype=jnp.float32)

    reach, saved = transit, written
    step = 1
    while step < blocks:
        earlier_reach = shift_down(reach, step, identity)
        earlier_saved = shift_down(saved, step, 0.0)
        saved = matrix_product(reach, earlier_saved) + saved
        reach = matrix_product(reach, earlier_reach)
        step *= 2

    place = lax.axis_index("z")
    group_reach, group_saved = reach[-1], saved[-1]
    step = 1
    while step < major:
        pairs = [(i, i + step) for i in range(major - step)]
        if 2 * step < major:
            got = lax.ppermute(jnp.stack([group_reach, group_saved]), "z", pairs)
            got_reach, got_saved = got[0], got[1]
            new_saved = matrix_product(group_reach, got_saved) + group_saved
            group_reach = jnp.where(
                place >= step, matrix_product(group_reach, got_reach), group_reach
            )
        else:
            got_saved = lax.ppermute(group_saved, "z", pairs)
            new_saved = matrix_product(group_reach, got_saved) + group_saved
        group_saved = new_saved
        step *= 2
    incoming = lax.ppermute(group_saved, "z", [(i, i + 1) for i in range(major - 1)])

    entry_reach = shift_down(reach, 1, identity)
    entry_saved = shift_down(saved, 1, 0.0)
    entry_state = matrix_product(entry_reach, incoming[None]) + entry_saved
    core_out = (
        jnp.einsum("bhcd,bhde->bhce", query_state, entry_state, precision=precise) + local_out
    )
    core_tokens = core_out.transpose(0, 2, 1, 3).reshape(tok_rows, local_heads, value_width)
    normed = gated_norm(
        core_tokens, gate_here.reshape(tok_rows, local_heads, value_width), norm_gain
    )
    normed = normed.reshape(tok_rows, local_heads * value_width)
    normed = lax.all_to_all(normed, "x", 0, 1, tiled=True)
    partial_value = jnp.dot(
        normed,
        lax.all_gather(out_weight, ("z", "x"), axis=1, tiled=True),
        preferred_element_type=jnp.float32,
    )
    return lax.psum_scatter(
        partial_value.astype(jnp.bfloat16), "heads", scatter_dimension=1, tiled=True
    )


def solution(mesh):
    heads_size, seq_size = mesh.devices.shape
    minor = SEQ_MINOR
    major = seq_size // minor
    split_mesh = Mesh(mesh.devices.reshape(heads_size, major, minor), ("heads", "z", "x"))
    seq = ("z", "x")
    placed = (
        P(seq, "heads"),
        P(seq, "heads"),
        P(seq, "heads"),
        P(seq, "heads"),
        P("heads", seq),
        P("heads", seq),
        P(seq),
        P(),
        P("heads", seq),
    )

    def body(*arrays):
        return on_device(*arrays, minor=minor, major=major)

    return jax.shard_map(
        body, mesh=split_mesh, in_specs=placed, out_specs=P(seq, "heads"), check_vma=False
    )
```

```python
import jax
import jax.numpy as jnp
from jax import lax
from jax.sharding import Mesh
from jax.sharding import PartitionSpec as P

STRETCH = 64
SEQ_MINOR = 4
SPLIT_GATHER = True
A2A_SCATTER = True


precise = lax.Precision.HIGHEST
epsilon = 1e-06


def unit_rows(block):
    return block / jnp.sqrt(jnp.sum(block * block, axis=-1, keepdims=True) + epsilon)


def triangular_inverse_below(system, right_side):
    return jax.scipy.linalg.solve_triangular(system, right_side, lower=True, unit_diagonal=True)


def matrix_product(left_side, right_side):
    return jnp.einsum("...de,...ef->...df", left_side, right_side, precision=precise)


def stretch_terms(queries, keys_normed, values_in, rates, decays, resets):
    length = queries.shape[-2]
    value_width = values_in.shape[-1]
    cumulated = jnp.cumsum(decays, axis=-1)
    seen = jnp.cumsum(resets, axis=-1)
    row_index = lax.broadcasted_iota(jnp.int32, (length, length), 0)
    col_index = lax.broadcasted_iota(jnp.int32, (length, length), 1)
    same_span = (seen[..., :, None] == seen[..., None, :]) & (row_index >= col_index)
    log_gap = jnp.where(same_span, cumulated[..., :, None] - cumulated[..., None, :], 0.0)
    pair_decay = jnp.where(same_span, jnp.exp(log_gap), 0.0)
    head_decay = jnp.exp(cumulated) * (seen == 0).astype(jnp.float32)
    tail_decay = jnp.exp(cumulated[..., -1:] - cumulated) * (seen[..., -1:] == seen).astype(
        jnp.float32
    )
    key_gram = jnp.einsum("...cd,...md->...cm", keys_normed, keys_normed, precision=precise)
    strict_part = jnp.where(row_index > col_index, rates[..., :, None] * pair_decay * key_gram, 0.0)
    system = strict_part + jnp.eye(length, dtype=jnp.float32)
    both_sides = jnp.concatenate(
        [rates[..., None] * values_in, (rates * head_decay)[..., None] * keys_normed], axis=-1
    )
    solved = triangular_inverse_below(system, both_sides)
    pseudo_values = solved[..., :value_width]
    key_weights = solved[..., value_width:]
    scores = pair_decay * jnp.einsum("...cd,...md->...cm", queries, keys_normed, precision=precise)
    query_state = head_decay[..., None] * queries - jnp.einsum(
        "...cm,...md->...cd", scores, key_weights, precision=precise
    )
    local_out = jnp.einsum("...cm,...md->...cd", scores, pseudo_values, precision=precise)
    identity = jnp.eye(keys_normed.shape[-1], dtype=jnp.float32)
    transit = head_decay[..., -1][..., None, None] * identity - jnp.einsum(
        "...cd,...ce->...de", keys_normed, tail_decay[..., None] * key_weights, precision=precise
    )
    written = jnp.einsum(
        "...cd,...ce->...de", keys_normed, tail_decay[..., None] * pseudo_values, precision=precise
    )
    return (query_state, local_out, transit, written)


def gated_norm(core_out, gate_block, gain):
    scale = lax.rsqrt(jnp.mean(core_out * core_out, axis=-1, keepdims=True) + epsilon)
    gate_float = gate_block.astype(jnp.float32)
    return (core_out * scale * gain * jax.nn.silu(gate_float)).astype(jnp.bfloat16)


def shift_down(array, step, fill):
    head = jnp.broadcast_to(fill, (step,) + array.shape[1:]).astype(array.dtype)
    return jnp.concatenate([head, array[:-step]], axis=0)


def on_device(
    query_proj,
    key_proj,
    value_proj,
    gate_proj,
    write_rate,
    log_decay,
    doc_start,
    norm_gain,
    out_weight,
    minor,
    major,
):
    head_count = write_rate.shape[0]
    key_width = query_proj.shape[1] // head_count
    value_width = value_proj.shape[1] // head_count

    projections = jnp.stack([query_proj, key_proj, value_proj, gate_proj])
    projections = lax.all_to_all(projections, "x", 2, 1, tiled=True)
    query_here, key_here, value_here, gate_here = (projections[i] for i in range(4))
    resets_wide = jnp.broadcast_to(doc_start.astype(jnp.float32), write_rate.shape)
    per_token = jnp.stack([write_rate, log_decay, resets_wide])
    per_token = lax.all_to_all(per_token, "x", 1, 2, tiled=True)
    rates_here, decays_here = per_token[0], per_token[1]
    resets_here = per_token[2, 0].astype(jnp.int32)

    tok_rows = query_here.shape[0]
    local_heads = head_count // minor
    blocks = tok_rows // STRETCH

    def stretch_major(array, width):
        return array.reshape(blocks, STRETCH, local_heads, width).transpose(0, 2, 1, 3)

    queries = unit_rows(stretch_major(query_here, key_width).astype(jnp.float32))
    keys_normed = unit_rows(stretch_major(key_here, key_width).astype(jnp.float32))
    values_in = stretch_major(value_here, value_width).astype(jnp.float32)
    rates = rates_here.reshape(local_heads, blocks, STRETCH).transpose(1, 0, 2)
    decays = decays_here.reshape(local_heads, blocks, STRETCH).transpose(1, 0, 2)
    resets = resets_here.reshape(blocks, 1, STRETCH)
    query_state, local_out, transit, written = stretch_terms(
        queries, keys_normed, values_in, rates, decays, resets
    )
    identity = jnp.eye(key_width, dtype=jnp.float32)

    reach, saved = transit, written
    step = 1
    while step < blocks:
        earlier_reach = shift_down(reach, step, identity)
        earlier_saved = shift_down(saved, step, 0.0)
        saved = matrix_product(reach, earlier_saved) + saved
        reach = matrix_product(reach, earlier_reach)
        step *= 2

    place = lax.axis_index("z")
    group_reach, group_saved = reach[-1], saved[-1]
    step = 1
    while step < major:
        pairs = [(i, i + step) for i in range(major - step)]
        if 2 * step < major:
            got = lax.ppermute(jnp.stack([group_reach, group_saved]), "z", pairs)
            got_reach, got_saved = got[0], got[1]
            new_saved = matrix_product(group_reach, got_saved) + group_saved
            group_reach = jnp.where(
                place >= step, matrix_product(group_reach, got_reach), group_reach
            )
        else:
            got_saved = lax.ppermute(group_saved, "z", pairs)
            new_saved = matrix_product(group_reach, got_saved) + group_saved
        group_saved = new_saved
        step *= 2
    incoming = lax.ppermute(group_saved, "z", [(i, i + 1) for i in range(major - 1)])

    entry_reach = shift_down(reach, 1, identity)
    entry_saved = shift_down(saved, 1, 0.0)
    entry_state = matrix_product(entry_reach, incoming[None]) + entry_saved
    core_out = (
        jnp.einsum("bhcd,bhde->bhce", query_state, entry_state, precision=precise) + local_out
    )
    core_tokens = core_out.transpose(0, 2, 1, 3).reshape(tok_rows, local_heads, value_width)
    normed = gated_norm(
        core_tokens, gate_here.reshape(tok_rows, local_heads, value_width), norm_gain
    )
    normed = normed.reshape(tok_rows, local_heads * value_width)
    normed = lax.all_to_all(normed, "x", 0, 1, tiled=True)
    if SPLIT_GATHER:
        weight_rows = lax.all_gather(out_weight, "z", axis=1, tiled=True)
        weight_rows = lax.all_gather(weight_rows, "x", axis=1, tiled=True)
        row_count, col_count = weight_rows.shape
        weight_rows = (
            weight_rows.reshape(row_count, minor, major, col_count // (minor * major))
            .transpose(0, 2, 1, 3)
            .reshape(row_count, col_count)
        )
    else:
        weight_rows = lax.all_gather(out_weight, ("z", "x"), axis=1, tiled=True)
    partial_value = jnp.dot(normed, weight_rows, preferred_element_type=jnp.float32)
    partial_value = partial_value.astype(jnp.bfloat16)
    if A2A_SCATTER:
        groups = lax.psum(1, "heads")
        pieces = partial_value.reshape(partial_value.shape[0], groups, -1)
        pieces = lax.all_to_all(pieces, "heads", 1, 1, tiled=True)
        return jnp.sum(pieces.astype(jnp.float32), axis=1).astype(jnp.bfloat16)
    return lax.psum_scatter(partial_value, "heads", scatter_dimension=1, tiled=True)


def solution(mesh):
    heads_size, seq_size = mesh.devices.shape
    minor = SEQ_MINOR
    major = seq_size // minor
    split_mesh = Mesh(mesh.devices.reshape(heads_size, major, minor), ("heads", "z", "x"))
    seq = ("z", "x")
    placed = (
        P(seq, "heads"),
        P(seq, "heads"),
        P(seq, "heads"),
        P(seq, "heads"),
        P("heads", seq),
        P("heads", seq),
        P(seq),
        P(),
        P("heads", seq),
    )

    def body(*arrays):
        return on_device(*arrays, minor=minor, major=major)

    return jax.shard_map(
        body, mesh=split_mesh, in_specs=placed, out_specs=P(seq, "heads"), check_vma=False
    )
```

```python
import jax
import jax.numpy as jnp
from jax import lax
from jax.sharding import Mesh
from jax.sharding import PartitionSpec as P

STRETCH = 64
SEQ_MINOR = 4
INVERSE_BASE = 16


precise = lax.Precision.HIGHEST
epsilon = 1e-06


def unit_rows(block):
    return block / jnp.sqrt(jnp.sum(block * block, axis=-1, keepdims=True) + epsilon)


def triangular_inverse_below(system, right_side):
    return matrix_product(unit_lower_inverse(system), right_side)


def matrix_product(left_side, right_side):
    return jnp.einsum("...de,...ef->...df", left_side, right_side, precision=precise)


def unit_lower_inverse(system):
    size = system.shape[-1]
    width = min(INVERSE_BASE, size)
    count = size // width
    identity = jnp.eye(width, dtype=system.dtype)
    diagonal = jnp.stack(
        [system[..., i * width : (i + 1) * width, i * width : (i + 1) * width] for i in range(count)],
        axis=-3,
    )
    nilpotent = identity - diagonal
    inverse = identity + nilpotent
    power = 2
    while power < width:
        nilpotent = matrix_product(nilpotent, nilpotent)
        inverse = matrix_product(inverse, identity + nilpotent)
        power *= 2
    while width < size:
        pairs = count // 2
        below = jnp.stack(
            [
                system[..., (2 * j + 1) * width : (2 * j + 2) * width, 2 * j * width : (2 * j + 1) * width]
                for j in range(pairs)
            ],
            axis=-3,
        )
        upper_inverse = inverse[..., 0::2, :, :]
        lower_inverse = inverse[..., 1::2, :, :]
        corner = -matrix_product(matrix_product(lower_inverse, below), upper_inverse)
        empty = jnp.zeros_like(upper_inverse)
        inverse = jnp.concatenate(
            [
                jnp.concatenate([upper_inverse, empty], axis=-1),
                jnp.concatenate([corner, lower_inverse], axis=-1),
            ],
            axis=-2,
        )
        width *= 2
        count = pairs
    return inverse[..., 0, :, :]


def stretch_terms(queries, keys_normed, values_in, rates, decays, resets):
    length = queries.shape[-2]
    value_width = values_in.shape[-1]
    cumulated = jnp.cumsum(decays, axis=-1)
    seen = jnp.cumsum(resets, axis=-1)
    row_index = lax.broadcasted_iota(jnp.int32, (length, length), 0)
    col_index = lax.broadcasted_iota(jnp.int32, (length, length), 1)
    same_span = (seen[..., :, None] == seen[..., None, :]) & (row_index >= col_index)
    log_gap = jnp.where(same_span, cumulated[..., :, None] - cumulated[..., None, :], 0.0)
    pair_decay = jnp.where(same_span, jnp.exp(log_gap), 0.0)
    head_decay = jnp.exp(cumulated) * (seen == 0).astype(jnp.float32)
    tail_decay = jnp.exp(cumulated[..., -1:] - cumulated) * (seen[..., -1:] == seen).astype(
        jnp.float32
    )
    key_gram = jnp.einsum("...cd,...md->...cm", keys_normed, keys_normed, precision=precise)
    strict_part = jnp.where(row_index > col_index, rates[..., :, None] * pair_decay * key_gram, 0.0)
    system = strict_part + jnp.eye(length, dtype=jnp.float32)
    both_sides = jnp.concatenate(
        [rates[..., None] * values_in, (rates * head_decay)[..., None] * keys_normed], axis=-1
    )
    solved = triangular_inverse_below(system, both_sides)
    pseudo_values = solved[..., :value_width]
    key_weights = solved[..., value_width:]
    scores = pair_decay * jnp.einsum("...cd,...md->...cm", queries, keys_normed, precision=precise)
    query_state = head_decay[..., None] * queries - jnp.einsum(
        "...cm,...md->...cd", scores, key_weights, precision=precise
    )
    local_out = jnp.einsum("...cm,...md->...cd", scores, pseudo_values, precision=precise)
    identity = jnp.eye(keys_normed.shape[-1], dtype=jnp.float32)
    transit = head_decay[..., -1][..., None, None] * identity - jnp.einsum(
        "...cd,...ce->...de", keys_normed, tail_decay[..., None] * key_weights, precision=precise
    )
    written = jnp.einsum(
        "...cd,...ce->...de", keys_normed, tail_decay[..., None] * pseudo_values, precision=precise
    )
    return (query_state, local_out, transit, written)


def gated_norm(core_out, gate_block, gain):
    scale = lax.rsqrt(jnp.mean(core_out * core_out, axis=-1, keepdims=True) + epsilon)
    gate_float = gate_block.astype(jnp.float32)
    return (core_out * scale * gain * jax.nn.silu(gate_float)).astype(jnp.bfloat16)


def shift_down(array, step, fill):
    head = jnp.broadcast_to(fill, (step,) + array.shape[1:]).astype(array.dtype)
    return jnp.concatenate([head, array[:-step]], axis=0)


def on_device(
    query_proj,
    key_proj,
    value_proj,
    gate_proj,
    write_rate,
    log_decay,
    doc_start,
    norm_gain,
    out_weight,
    minor,
    major,
):
    head_count = write_rate.shape[0]
    key_width = query_proj.shape[1] // head_count
    value_width = value_proj.shape[1] // head_count

    projections = jnp.stack([query_proj, key_proj, value_proj, gate_proj])
    projections = lax.all_to_all(projections, "x", 2, 1, tiled=True)
    query_here, key_here, value_here, gate_here = (projections[i] for i in range(4))
    resets_wide = jnp.broadcast_to(doc_start.astype(jnp.float32), write_rate.shape)
    per_token = jnp.stack([write_rate, log_decay, resets_wide])
    per_token = lax.all_to_all(per_token, "x", 1, 2, tiled=True)
    rates_here, decays_here = per_token[0], per_token[1]
    resets_here = per_token[2, 0].astype(jnp.int32)

    tok_rows = query_here.shape[0]
    local_heads = head_count // minor
    blocks = tok_rows // STRETCH

    def stretch_major(array, width):
        return array.reshape(blocks, STRETCH, local_heads, width).transpose(0, 2, 1, 3)

    queries = unit_rows(stretch_major(query_here, key_width).astype(jnp.float32))
    keys_normed = unit_rows(stretch_major(key_here, key_width).astype(jnp.float32))
    values_in = stretch_major(value_here, value_width).astype(jnp.float32)
    rates = rates_here.reshape(local_heads, blocks, STRETCH).transpose(1, 0, 2)
    decays = decays_here.reshape(local_heads, blocks, STRETCH).transpose(1, 0, 2)
    resets = resets_here.reshape(blocks, 1, STRETCH)
    query_state, local_out, transit, written = stretch_terms(
        queries, keys_normed, values_in, rates, decays, resets
    )
    identity = jnp.eye(key_width, dtype=jnp.float32)

    reach, saved = transit, written
    step = 1
    while step < blocks:
        earlier_reach = shift_down(reach, step, identity)
        earlier_saved = shift_down(saved, step, 0.0)
        saved = matrix_product(reach, earlier_saved) + saved
        reach = matrix_product(reach, earlier_reach)
        step *= 2

    place = lax.axis_index("z")
    group_reach, group_saved = reach[-1], saved[-1]
    step = 1
    while step < major:
        pairs = [(i, i + step) for i in range(major - step)]
        if 2 * step < major:
            got = lax.ppermute(jnp.stack([group_reach, group_saved]), "z", pairs)
            got_reach, got_saved = got[0], got[1]
            new_saved = matrix_product(group_reach, got_saved) + group_saved
            group_reach = jnp.where(
                place >= step, matrix_product(group_reach, got_reach), group_reach
            )
        else:
            got_saved = lax.ppermute(group_saved, "z", pairs)
            new_saved = matrix_product(group_reach, got_saved) + group_saved
        group_saved = new_saved
        step *= 2
    incoming = lax.ppermute(group_saved, "z", [(i, i + 1) for i in range(major - 1)])

    entry_reach = shift_down(reach, 1, identity)
    entry_saved = shift_down(saved, 1, 0.0)
    entry_state = matrix_product(entry_reach, incoming[None]) + entry_saved
    core_out = (
        jnp.einsum("bhcd,bhde->bhce", query_state, entry_state, precision=precise) + local_out
    )
    core_tokens = core_out.transpose(0, 2, 1, 3).reshape(tok_rows, local_heads, value_width)
    normed = gated_norm(
        core_tokens, gate_here.reshape(tok_rows, local_heads, value_width), norm_gain
    )
    normed = normed.reshape(tok_rows, local_heads * value_width)
    normed = lax.all_gather(normed, "x", axis=1, tiled=True)
    groups = lax.psum(1, "heads")
    weight_rows = lax.all_gather(out_weight, "z", axis=1, tiled=True)
    partial_value = jnp.dot(normed, weight_rows, preferred_element_type=jnp.float32)
    partial_value = partial_value.astype(jnp.bfloat16)
    rows = tok_rows // minor
    pieces = partial_value.reshape(minor, rows, groups, major // groups, -1)
    pieces = lax.all_to_all(pieces, "heads", 2, 2, tiled=True)
    summed = jnp.sum(pieces.astype(jnp.float32), axis=2).astype(jnp.bfloat16)
    summed = lax.all_to_all(summed, "x", 0, 0, tiled=True)
    return summed.transpose(1, 2, 0, 3).reshape(rows, -1)


def solution(mesh):
    heads_size, seq_size = mesh.devices.shape
    minor = SEQ_MINOR
    major = seq_size // minor
    split_mesh = Mesh(mesh.devices.reshape(heads_size, major, minor), ("heads", "z", "x"))
    seq = ("z", "x")
    placed = (
        P(seq, "heads"),
        P(seq, "heads"),
        P(seq, "heads"),
        P(seq, "heads"),
        P("heads", seq),
        P("heads", seq),
        P(seq),
        P(),
        P("heads", seq),
    )

    def body(*arrays):
        return on_device(*arrays, minor=minor, major=major)

    return jax.shard_map(
        body, mesh=split_mesh, in_specs=placed, out_specs=P(seq, "heads"), check_vma=False
    )
```

```python
import jax
import jax.numpy as jnp
from jax import lax
from jax.sharding import Mesh
from jax.sharding import PartitionSpec as P

STRETCH = 64
SEQ_MINOR = 4
INVERSE_BASE = 16
GATHER_AS_A2A = True
JOINT_A2A = True


precise = lax.Precision.HIGHEST
epsilon = 1e-06


def unit_rows(block):
    return block / jnp.sqrt(jnp.sum(block * block, axis=-1, keepdims=True) + epsilon)


def triangular_inverse_below(system, right_side):
    return matrix_product(unit_lower_inverse(system), right_side)


def matrix_product(left_side, right_side):
    return jnp.einsum("...de,...ef->...df", left_side, right_side, precision=precise)


def unit_lower_inverse(system):
    size = system.shape[-1]
    width = min(INVERSE_BASE, size)
    count = size // width
    identity = jnp.eye(width, dtype=system.dtype)
    diagonal = jnp.stack(
        [system[..., i * width : (i + 1) * width, i * width : (i + 1) * width] for i in range(count)],
        axis=-3,
    )
    nilpotent = identity - diagonal
    inverse = identity + nilpotent
    power = 2
    while power < width:
        nilpotent = matrix_product(nilpotent, nilpotent)
        inverse = matrix_product(inverse, identity + nilpotent)
        power *= 2
    while width < size:
        pairs = count // 2
        below = jnp.stack(
            [
                system[..., (2 * j + 1) * width : (2 * j + 2) * width, 2 * j * width : (2 * j + 1) * width]
                for j in range(pairs)
            ],
            axis=-3,
        )
        upper_inverse = inverse[..., 0::2, :, :]
        lower_inverse = inverse[..., 1::2, :, :]
        corner = -matrix_product(matrix_product(lower_inverse, below), upper_inverse)
        empty = jnp.zeros_like(upper_inverse)
        inverse = jnp.concatenate(
            [
                jnp.concatenate([upper_inverse, empty], axis=-1),
                jnp.concatenate([corner, lower_inverse], axis=-1),
            ],
            axis=-2,
        )
        width *= 2
        count = pairs
    return inverse[..., 0, :, :]


def stretch_terms(queries, keys_normed, values_in, rates, decays, resets):
    length = queries.shape[-2]
    value_width = values_in.shape[-1]
    cumulated = jnp.cumsum(decays, axis=-1)
    seen = jnp.cumsum(resets, axis=-1)
    row_index = lax.broadcasted_iota(jnp.int32, (length, length), 0)
    col_index = lax.broadcasted_iota(jnp.int32, (length, length), 1)
    same_span = (seen[..., :, None] == seen[..., None, :]) & (row_index >= col_index)
    log_gap = jnp.where(same_span, cumulated[..., :, None] - cumulated[..., None, :], 0.0)
    pair_decay = jnp.where(same_span, jnp.exp(log_gap), 0.0)
    head_decay = jnp.exp(cumulated) * (seen == 0).astype(jnp.float32)
    tail_decay = jnp.exp(cumulated[..., -1:] - cumulated) * (seen[..., -1:] == seen).astype(
        jnp.float32
    )
    key_gram = jnp.einsum("...cd,...md->...cm", keys_normed, keys_normed, precision=precise)
    strict_part = jnp.where(row_index > col_index, rates[..., :, None] * pair_decay * key_gram, 0.0)
    system = strict_part + jnp.eye(length, dtype=jnp.float32)
    both_sides = jnp.concatenate(
        [rates[..., None] * values_in, (rates * head_decay)[..., None] * keys_normed], axis=-1
    )
    solved = triangular_inverse_below(system, both_sides)
    pseudo_values = solved[..., :value_width]
    key_weights = solved[..., value_width:]
    scores = pair_decay * jnp.einsum("...cd,...md->...cm", queries, keys_normed, precision=precise)
    query_state = head_decay[..., None] * queries - jnp.einsum(
        "...cm,...md->...cd", scores, key_weights, precision=precise
    )
    local_out = jnp.einsum("...cm,...md->...cd", scores, pseudo_values, precision=precise)
    identity = jnp.eye(keys_normed.shape[-1], dtype=jnp.float32)
    transit = head_decay[..., -1][..., None, None] * identity - jnp.einsum(
        "...cd,...ce->...de", keys_normed, tail_decay[..., None] * key_weights, precision=precise
    )
    written = jnp.einsum(
        "...cd,...ce->...de", keys_normed, tail_decay[..., None] * pseudo_values, precision=precise
    )
    return (query_state, local_out, transit, written)


def gated_norm(core_out, gate_block, gain):
    scale = lax.rsqrt(jnp.mean(core_out * core_out, axis=-1, keepdims=True) + epsilon)
    gate_float = gate_block.astype(jnp.float32)
    return (core_out * scale * gain * jax.nn.silu(gate_float)).astype(jnp.bfloat16)


def shift_down(array, step, fill):
    head = jnp.broadcast_to(fill, (step,) + array.shape[1:]).astype(array.dtype)
    return jnp.concatenate([head, array[:-step]], axis=0)


def on_device(
    query_proj,
    key_proj,
    value_proj,
    gate_proj,
    write_rate,
    log_decay,
    doc_start,
    norm_gain,
    out_weight,
    minor,
    major,
):
    head_count = write_rate.shape[0]
    key_width = query_proj.shape[1] // head_count
    value_width = value_proj.shape[1] // head_count

    projections = jnp.stack([query_proj, key_proj, value_proj, gate_proj])
    projections = lax.all_to_all(projections, "x", 2, 1, tiled=True)
    query_here, key_here, value_here, gate_here = (projections[i] for i in range(4))
    resets_wide = jnp.broadcast_to(doc_start.astype(jnp.float32), write_rate.shape)
    per_token = jnp.stack([write_rate, log_decay, resets_wide])
    per_token = lax.all_to_all(per_token, "x", 1, 2, tiled=True)
    rates_here, decays_here = per_token[0], per_token[1]
    resets_here = per_token[2, 0].astype(jnp.int32)

    tok_rows = query_here.shape[0]
    local_heads = head_count // minor
    blocks = tok_rows // STRETCH

    def stretch_major(array, width):
        return array.reshape(blocks, STRETCH, local_heads, width).transpose(0, 2, 1, 3)

    queries = unit_rows(stretch_major(query_here, key_width).astype(jnp.float32))
    keys_normed = unit_rows(stretch_major(key_here, key_width).astype(jnp.float32))
    values_in = stretch_major(value_here, value_width).astype(jnp.float32)
    rates = rates_here.reshape(local_heads, blocks, STRETCH).transpose(1, 0, 2)
    decays = decays_here.reshape(local_heads, blocks, STRETCH).transpose(1, 0, 2)
    resets = resets_here.reshape(blocks, 1, STRETCH)
    query_state, local_out, transit, written = stretch_terms(
        queries, keys_normed, values_in, rates, decays, resets
    )
    identity = jnp.eye(key_width, dtype=jnp.float32)

    reach, saved = transit, written
    step = 1
    while step < blocks:
        earlier_reach = shift_down(reach, step, identity)
        earlier_saved = shift_down(saved, step, 0.0)
        saved = matrix_product(reach, earlier_saved) + saved
        reach = matrix_product(reach, earlier_reach)
        step *= 2

    place = lax.axis_index("z")
    group_reach, group_saved = reach[-1], saved[-1]
    step = 1
    while step < major:
        pairs = [(i, i + step) for i in range(major - step)]
        if 2 * step < major:
            got = lax.ppermute(jnp.stack([group_reach, group_saved]), "z", pairs)
            got_reach, got_saved = got[0], got[1]
            new_saved = matrix_product(group_reach, got_saved) + group_saved
            group_reach = jnp.where(
                place >= step, matrix_product(group_reach, got_reach), group_reach
            )
        else:
            got_saved = lax.ppermute(group_saved, "z", pairs)
            new_saved = matrix_product(group_reach, got_saved) + group_saved
        group_saved = new_saved
        step *= 2
    incoming = lax.ppermute(group_saved, "z", [(i, i + 1) for i in range(major - 1)])

    entry_reach = shift_down(reach, 1, identity)
    entry_saved = shift_down(saved, 1, 0.0)
    entry_state = matrix_product(entry_reach, incoming[None]) + entry_saved
    core_out = (
        jnp.einsum("bhcd,bhde->bhce", query_state, entry_state, precision=precise) + local_out
    )
    core_tokens = core_out.transpose(0, 2, 1, 3).reshape(tok_rows, local_heads, value_width)
    normed = gated_norm(
        core_tokens, gate_here.reshape(tok_rows, local_heads, value_width), norm_gain
    )
    normed = normed.reshape(tok_rows, local_heads * value_width)
    if GATHER_AS_A2A:
        copies = jnp.broadcast_to(normed[None], (minor,) + normed.shape)
        normed = lax.all_to_all(copies, "x", 0, 0, tiled=True)
        normed = normed.transpose(1, 0, 2).reshape(tok_rows, -1)
    else:
        normed = lax.all_gather(normed, "x", axis=1, tiled=True)
    groups = lax.psum(1, "heads")
    weight_rows = lax.all_gather(out_weight, "z", axis=1, tiled=True)
    partial_value = jnp.dot(normed, weight_rows, preferred_element_type=jnp.float32)
    partial_value = partial_value.astype(jnp.bfloat16)
    rows = tok_rows // minor
    pieces = partial_value.reshape(minor, rows, groups, major // groups, -1)
    if JOINT_A2A:
        pieces = pieces.transpose(0, 2, 1, 3, 4).reshape(minor * groups, rows, major // groups, -1)
        pieces = lax.all_to_all(pieces, ("x", "heads"), 0, 0, tiled=True)
        pieces = pieces.reshape(minor, groups, rows, major // groups, -1)
        summed = jnp.sum(pieces.astype(jnp.float32), axis=1).astype(jnp.bfloat16)
    else:
        pieces = lax.all_to_all(pieces, "heads", 2, 2, tiled=True)
        summed = jnp.sum(pieces.astype(jnp.float32), axis=2).astype(jnp.bfloat16)
        summed = lax.all_to_all(summed, "x", 0, 0, tiled=True)
    return summed.transpose(1, 2, 0, 3).reshape(rows, -1)


def solution(mesh):
    heads_size, seq_size = mesh.devices.shape
    minor = SEQ_MINOR
    major = seq_size // minor
    split_mesh = Mesh(mesh.devices.reshape(heads_size, major, minor), ("heads", "z", "x"))
    seq = ("z", "x")
    placed = (
        P(seq, "heads"),
        P(seq, "heads"),
        P(seq, "heads"),
        P(seq, "heads"),
        P("heads", seq),
        P("heads", seq),
        P(seq),
        P(),
        P("heads", seq),
    )

    def body(*arrays):
        return on_device(*arrays, minor=minor, major=major)

    return jax.shard_map(
        body, mesh=split_mesh, in_specs=placed, out_specs=P(seq, "heads"), check_vma=False
    )
```

```python
import jax
import jax.numpy as jnp
from jax import lax
from jax.sharding import Mesh
from jax.sharding import PartitionSpec as P

STRETCH = 64
SEQ_MINOR = 4
INVERSE_BASE = 16
GATHER_AS_A2A = True
JOINT_A2A = True


precise = lax.Precision.HIGHEST
epsilon = 1e-06


def unit_rows(block):
    return block / jnp.sqrt(jnp.sum(block * block, axis=-1, keepdims=True) + epsilon)


def triangular_inverse_below(system, right_side):
    return matrix_product(unit_lower_inverse(system), right_side)


def matrix_product(left_side, right_side):
    return jnp.einsum("...de,...ef->...df", left_side, right_side, precision=precise)


def unit_lower_inverse(system):
    size = system.shape[-1]
    width = min(INVERSE_BASE, size)
    count = size // width
    identity = jnp.eye(width, dtype=system.dtype)
    diagonal = jnp.stack(
        [system[..., i * width : (i + 1) * width, i * width : (i + 1) * width] for i in range(count)],
        axis=-3,
    )
    nilpotent = identity - diagonal
    inverse = identity + nilpotent
    power = 2
    while power < width:
        nilpotent = matrix_product(nilpotent, nilpotent)
        inverse = matrix_product(inverse, identity + nilpotent)
        power *= 2
    while width < size:
        pairs = count // 2
        below = jnp.stack(
            [
                system[..., (2 * j + 1) * width : (2 * j + 2) * width, 2 * j * width : (2 * j + 1) * width]
                for j in range(pairs)
            ],
            axis=-3,
        )
        upper_inverse = inverse[..., 0::2, :, :]
        lower_inverse = inverse[..., 1::2, :, :]
        corner = -matrix_product(matrix_product(lower_inverse, below), upper_inverse)
        empty = jnp.zeros_like(upper_inverse)
        inverse = jnp.concatenate(
            [
                jnp.concatenate([upper_inverse, empty], axis=-1),
                jnp.concatenate([corner, lower_inverse], axis=-1),
            ],
            axis=-2,
        )
        width *= 2
        count = pairs
    return inverse[..., 0, :, :]


def stretch_terms(queries, keys_normed, values_in, rates, decays, resets):
    length = queries.shape[-2]
    value_width = values_in.shape[-1]
    cumulated = jnp.cumsum(decays, axis=-1)
    seen = jnp.cumsum(resets, axis=-1)
    row_index = lax.broadcasted_iota(jnp.int32, (length, length), 0)
    col_index = lax.broadcasted_iota(jnp.int32, (length, length), 1)
    same_span = (seen[..., :, None] == seen[..., None, :]) & (row_index >= col_index)
    log_gap = jnp.where(same_span, cumulated[..., :, None] - cumulated[..., None, :], 0.0)
    pair_decay = jnp.where(same_span, jnp.exp(log_gap), 0.0)
    head_decay = jnp.exp(cumulated) * (seen == 0).astype(jnp.float32)
    tail_decay = jnp.exp(cumulated[..., -1:] - cumulated) * (seen[..., -1:] == seen).astype(
        jnp.float32
    )
    key_gram = jnp.einsum("...cd,...md->...cm", keys_normed, keys_normed, precision=precise)
    strict_part = jnp.where(row_index > col_index, rates[..., :, None] * pair_decay * key_gram, 0.0)
    system = strict_part + jnp.eye(length, dtype=jnp.float32)
    both_sides = jnp.concatenate(
        [rates[..., None] * values_in, (rates * head_decay)[..., None] * keys_normed], axis=-1
    )
    solved = triangular_inverse_below(system, both_sides)
    pseudo_values = solved[..., :value_width]
    key_weights = solved[..., value_width:]
    scores = pair_decay * jnp.einsum("...cd,...md->...cm", queries, keys_normed, precision=precise)
    query_state = head_decay[..., None] * queries - jnp.einsum(
        "...cm,...md->...cd", scores, key_weights, precision=precise
    )
    local_out = jnp.einsum("...cm,...md->...cd", scores, pseudo_values, precision=precise)
    identity = jnp.eye(keys_normed.shape[-1], dtype=jnp.float32)
    transit = head_decay[..., -1][..., None, None] * identity - jnp.einsum(
        "...cd,...ce->...de", keys_normed, tail_decay[..., None] * key_weights, precision=precise
    )
    written = jnp.einsum(
        "...cd,...ce->...de", keys_normed, tail_decay[..., None] * pseudo_values, precision=precise
    )
    return (query_state, local_out, transit, written)


def gated_norm(core_out, gate_block, gain):
    scale = lax.rsqrt(jnp.mean(core_out * core_out, axis=-1, keepdims=True) + epsilon)
    gate_float = gate_block.astype(jnp.float32)
    return (core_out * scale * gain * jax.nn.silu(gate_float)).astype(jnp.bfloat16)


def shift_down(array, step, fill):
    head = jnp.broadcast_to(fill, (step,) + array.shape[1:]).astype(array.dtype)
    return jnp.concatenate([head, array[:-step]], axis=0)


def on_device(
    query_proj,
    key_proj,
    value_proj,
    gate_proj,
    write_rate,
    log_decay,
    doc_start,
    norm_gain,
    out_weight,
    minor,
    major,
):
    head_count = write_rate.shape[0]
    key_width = query_proj.shape[1] // head_count
    value_width = value_proj.shape[1] // head_count

    local_rows = query_proj.shape[0]
    local_heads = head_count // minor
    resets_wide = jnp.broadcast_to(doc_start.astype(jnp.float32), write_rate.shape)
    per_token = jnp.stack([write_rate, log_decay, resets_wide])
    high = lax.optimization_barrier(per_token.astype(jnp.bfloat16))
    rest = per_token - high.astype(jnp.float32)
    middle = lax.optimization_barrier(rest.astype(jnp.bfloat16))
    low = (rest - middle.astype(jnp.float32)).astype(jnp.bfloat16)
    exact_parts = jnp.concatenate([high, middle, low])
    exact_parts = exact_parts.reshape(9, minor, local_heads, local_rows).transpose(3, 1, 0, 2)
    exact_parts = exact_parts.reshape(local_rows, minor, 9 * local_heads)
    projections = jnp.stack([query_proj, key_proj, value_proj, gate_proj], axis=1)
    projections = projections.reshape(local_rows, 4, minor, -1).transpose(0, 2, 1, 3)
    projections = projections.reshape(local_rows, minor, -1)
    width = projections.shape[-1]
    moved = jnp.concatenate([projections, exact_parts], axis=-1)
    moved = lax.all_to_all(moved, "x", 1, 0, tiled=True)
    moved = moved.reshape(minor * local_rows, -1)
    projections = moved[:, :width].reshape(minor * local_rows, 4, -1)
    query_here, key_here, value_here, gate_here = (projections[:, i] for i in range(4))
    exact_parts = moved[:, width:].astype(jnp.float32).reshape(minor * local_rows, 3, 3, local_heads)
    per_token = (exact_parts[:, 0] + exact_parts[:, 1]) + exact_parts[:, 2]
    per_token = per_token.transpose(1, 2, 0)
    rates_here, decays_here = per_token[0], per_token[1]
    resets_here = per_token[2, 0].astype(jnp.int32)

    tok_rows = query_here.shape[0]
    blocks = tok_rows // STRETCH

    def stretch_major(array, width):
        return array.reshape(blocks, STRETCH, local_heads, width).transpose(0, 2, 1, 3)

    queries = unit_rows(stretch_major(query_here, key_width).astype(jnp.float32))
    keys_normed = unit_rows(stretch_major(key_here, key_width).astype(jnp.float32))
    values_in = stretch_major(value_here, value_width).astype(jnp.float32)
    rates = rates_here.reshape(local_heads, blocks, STRETCH).transpose(1, 0, 2)
    decays = decays_here.reshape(local_heads, blocks, STRETCH).transpose(1, 0, 2)
    resets = resets_here.reshape(blocks, 1, STRETCH)
    query_state, local_out, transit, written = stretch_terms(
        queries, keys_normed, values_in, rates, decays, resets
    )
    identity = jnp.eye(key_width, dtype=jnp.float32)

    reach, saved = transit, written
    step = 1
    while step < blocks:
        earlier_reach = shift_down(reach, step, identity)
        earlier_saved = shift_down(saved, step, 0.0)
        saved = matrix_product(reach, earlier_saved) + saved
        reach = matrix_product(reach, earlier_reach)
        step *= 2

    place = lax.axis_index("z")
    group_reach, group_saved = reach[-1], saved[-1]
    step = 1
    while step < major:
        pairs = [(i, i + step) for i in range(major - step)]
        if 2 * step < major:
            got = lax.ppermute(jnp.stack([group_reach, group_saved]), "z", pairs)
            got_reach, got_saved = got[0], got[1]
            new_saved = matrix_product(group_reach, got_saved) + group_saved
            group_reach = jnp.where(
                place >= step, matrix_product(group_reach, got_reach), group_reach
            )
        else:
            got_saved = lax.ppermute(group_saved, "z", pairs)
            new_saved = matrix_product(group_reach, got_saved) + group_saved
        group_saved = new_saved
        step *= 2
    incoming = lax.ppermute(group_saved, "z", [(i, i + 1) for i in range(major - 1)])

    entry_reach = shift_down(reach, 1, identity)
    entry_saved = shift_down(saved, 1, 0.0)
    entry_state = matrix_product(entry_reach, incoming[None]) + entry_saved
    core_out = (
        jnp.einsum("bhcd,bhde->bhce", query_state, entry_state, precision=precise) + local_out
    )
    core_tokens = core_out.transpose(0, 2, 1, 3).reshape(tok_rows, local_heads, value_width)
    normed = gated_norm(
        core_tokens, gate_here.reshape(tok_rows, local_heads, value_width), norm_gain
    )
    normed = normed.reshape(tok_rows, local_heads * value_width)
    if GATHER_AS_A2A:
        copies = jnp.broadcast_to(normed[None], (minor,) + normed.shape)
        normed = lax.all_to_all(copies, "x", 0, 0, tiled=True)
        normed = normed.transpose(1, 0, 2).reshape(tok_rows, -1)
    else:
        normed = lax.all_gather(normed, "x", axis=1, tiled=True)
    groups = lax.psum(1, "heads")
    weight_rows = lax.all_gather(out_weight, "z", axis=1, tiled=True)
    partial_value = jnp.dot(normed, weight_rows, preferred_element_type=jnp.float32)
    partial_value = partial_value.astype(jnp.bfloat16)
    rows = tok_rows // minor
    pieces = partial_value.reshape(minor, rows, groups, major // groups, -1)
    if JOINT_A2A:
        pieces = pieces.transpose(0, 2, 1, 3, 4).reshape(minor * groups, rows, major // groups, -1)
        pieces = lax.all_to_all(pieces, ("x", "heads"), 0, 0, tiled=True)
        pieces = pieces.reshape(minor, groups, rows, major // groups, -1)
        summed = jnp.sum(pieces.astype(jnp.float32), axis=1).astype(jnp.bfloat16)
    else:
        pieces = lax.all_to_all(pieces, "heads", 2, 2, tiled=True)
        summed = jnp.sum(pieces.astype(jnp.float32), axis=2).astype(jnp.bfloat16)
        summed = lax.all_to_all(summed, "x", 0, 0, tiled=True)
    return summed.transpose(1, 2, 0, 3).reshape(rows, -1)


def solution(mesh):
    heads_size, seq_size = mesh.devices.shape
    minor = SEQ_MINOR
    major = seq_size // minor
    split_mesh = Mesh(mesh.devices.reshape(heads_size, major, minor), ("heads", "z", "x"))
    seq = ("z", "x")
    placed = (
        P(seq, "heads"),
        P(seq, "heads"),
        P(seq, "heads"),
        P(seq, "heads"),
        P("heads", seq),
        P("heads", seq),
        P(seq),
        P(),
        P("heads", seq),
    )

    def body(*arrays):
        return on_device(*arrays, minor=minor, major=major)

    return jax.shard_map(
        body, mesh=split_mesh, in_specs=placed, out_specs=P(seq, "heads"), check_vma=False
    )
```

```python
import jax
import jax.numpy as jnp
from jax import lax
from jax.sharding import Mesh
from jax.sharding import PartitionSpec as P

STRETCH = 64
SEQ_MINOR = 4
INVERSE_BASE = 16
GATHER_AS_A2A = True
JOINT_A2A = True


precise = lax.Precision.HIGH
epsilon = 1e-06


def unit_rows(block):
    return block / jnp.sqrt(jnp.sum(block * block, axis=-1, keepdims=True) + epsilon)


def triangular_inverse_below(system, right_side):
    return matrix_product(unit_lower_inverse(system), right_side)


def matrix_product(left_side, right_side):
    return jnp.einsum("...de,...ef->...df", left_side, right_side, precision=precise)


def unit_lower_inverse(system):
    size = system.shape[-1]
    width = min(INVERSE_BASE, size)
    count = size // width
    identity = jnp.eye(width, dtype=system.dtype)
    diagonal = jnp.stack(
        [system[..., i * width : (i + 1) * width, i * width : (i + 1) * width] for i in range(count)],
        axis=-3,
    )
    nilpotent = identity - diagonal
    inverse = identity + nilpotent
    power = 2
    while power < width:
        nilpotent = matrix_product(nilpotent, nilpotent)
        inverse = matrix_product(inverse, identity + nilpotent)
        power *= 2
    while width < size:
        pairs = count // 2
        below = jnp.stack(
            [
                system[..., (2 * j + 1) * width : (2 * j + 2) * width, 2 * j * width : (2 * j + 1) * width]
                for j in range(pairs)
            ],
            axis=-3,
        )
        upper_inverse = inverse[..., 0::2, :, :]
        lower_inverse = inverse[..., 1::2, :, :]
        corner = -matrix_product(matrix_product(lower_inverse, below), upper_inverse)
        empty = jnp.zeros_like(upper_inverse)
        inverse = jnp.concatenate(
            [
                jnp.concatenate([upper_inverse, empty], axis=-1),
                jnp.concatenate([corner, lower_inverse], axis=-1),
            ],
            axis=-2,
        )
        width *= 2
        count = pairs
    return inverse[..., 0, :, :]


def stretch_terms(queries, keys_normed, values_in, rates, decays, resets):
    length = queries.shape[-2]
    value_width = values_in.shape[-1]
    cumulated = jnp.cumsum(decays, axis=-1)
    seen = jnp.cumsum(resets, axis=-1)
    row_index = lax.broadcasted_iota(jnp.int32, (length, length), 0)
    col_index = lax.broadcasted_iota(jnp.int32, (length, length), 1)
    same_span = (seen[..., :, None] == seen[..., None, :]) & (row_index >= col_index)
    log_gap = jnp.where(same_span, cumulated[..., :, None] - cumulated[..., None, :], 0.0)
    pair_decay = jnp.where(same_span, jnp.exp(log_gap), 0.0)
    head_decay = jnp.exp(cumulated) * (seen == 0).astype(jnp.float32)
    tail_decay = jnp.exp(cumulated[..., -1:] - cumulated) * (seen[..., -1:] == seen).astype(
        jnp.float32
    )
    key_gram = jnp.einsum("...cd,...md->...cm", keys_normed, keys_normed, precision=precise)
    strict_part = jnp.where(row_index > col_index, rates[..., :, None] * pair_decay * key_gram, 0.0)
    system = strict_part + jnp.eye(length, dtype=jnp.float32)
    both_sides = jnp.concatenate(
        [rates[..., None] * values_in, (rates * head_decay)[..., None] * keys_normed], axis=-1
    )
    solved = triangular_inverse_below(system, both_sides)
    pseudo_values = solved[..., :value_width]
    key_weights = solved[..., value_width:]
    scores = pair_decay * jnp.einsum("...cd,...md->...cm", queries, keys_normed, precision=precise)
    query_state = head_decay[..., None] * queries - jnp.einsum(
        "...cm,...md->...cd", scores, key_weights, precision=precise
    )
    local_out = jnp.einsum("...cm,...md->...cd", scores, pseudo_values, precision=precise)
    identity = jnp.eye(keys_normed.shape[-1], dtype=jnp.float32)
    transit = head_decay[..., -1][..., None, None] * identity - jnp.einsum(
        "...cd,...ce->...de", keys_normed, tail_decay[..., None] * key_weights, precision=precise
    )
    written = jnp.einsum(
        "...cd,...ce->...de", keys_normed, tail_decay[..., None] * pseudo_values, precision=precise
    )
    return (query_state, local_out, transit, written)


def gated_norm(core_out, gate_block, gain):
    scale = lax.rsqrt(jnp.mean(core_out * core_out, axis=-1, keepdims=True) + epsilon)
    gate_float = gate_block.astype(jnp.float32)
    return (core_out * scale * gain * jax.nn.silu(gate_float)).astype(jnp.bfloat16)


def shift_down(array, step, fill):
    head = jnp.broadcast_to(fill, (step,) + array.shape[1:]).astype(array.dtype)
    return jnp.concatenate([head, array[:-step]], axis=0)


def on_device(
    query_proj,
    key_proj,
    value_proj,
    gate_proj,
    write_rate,
    log_decay,
    doc_start,
    norm_gain,
    out_weight,
    minor,
    major,
):
    head_count = write_rate.shape[0]
    key_width = query_proj.shape[1] // head_count
    value_width = value_proj.shape[1] // head_count

    projections = jnp.stack([query_proj, key_proj, value_proj, gate_proj])
    projections = lax.all_to_all(projections, "x", 2, 1, tiled=True)
    query_here, key_here, value_here, gate_here = (projections[i] for i in range(4))
    resets_wide = jnp.broadcast_to(doc_start.astype(jnp.float32), write_rate.shape)
    per_token = jnp.stack([write_rate, log_decay, resets_wide])
    per_token = lax.all_to_all(per_token, "x", 1, 2, tiled=True)
    rates_here, decays_here = per_token[0], per_token[1]
    resets_here = per_token[2, 0].astype(jnp.int32)

    tok_rows = query_here.shape[0]
    local_heads = head_count // minor
    blocks = tok_rows // STRETCH

    def stretch_major(array, width):
        return array.reshape(blocks, STRETCH, local_heads, width).transpose(0, 2, 1, 3)

    queries = unit_rows(stretch_major(query_here, key_width).astype(jnp.float32))
    keys_normed = unit_rows(stretch_major(key_here, key_width).astype(jnp.float32))
    values_in = stretch_major(value_here, value_width).astype(jnp.float32)
    rates = rates_here.reshape(local_heads, blocks, STRETCH).transpose(1, 0, 2)
    decays = decays_here.reshape(local_heads, blocks, STRETCH).transpose(1, 0, 2)
    resets = resets_here.reshape(blocks, 1, STRETCH)
    query_state, local_out, transit, written = stretch_terms(
        queries, keys_normed, values_in, rates, decays, resets
    )
    identity = jnp.eye(key_width, dtype=jnp.float32)

    reach, saved = transit, written
    step = 1
    while step < blocks:
        earlier_reach = shift_down(reach, step, identity)
        earlier_saved = shift_down(saved, step, 0.0)
        saved = matrix_product(reach, earlier_saved) + saved
        reach = matrix_product(reach, earlier_reach)
        step *= 2

    place = lax.axis_index("z")
    group_reach, group_saved = reach[-1], saved[-1]
    step = 1
    while step < major:
        pairs = [(i, i + step) for i in range(major - step)]
        if 2 * step < major:
            got = lax.ppermute(jnp.stack([group_reach, group_saved]), "z", pairs)
            got_reach, got_saved = got[0], got[1]
            new_saved = matrix_product(group_reach, got_saved) + group_saved
            group_reach = jnp.where(
                place >= step, matrix_product(group_reach, got_reach), group_reach
            )
        else:
            got_saved = lax.ppermute(group_saved, "z", pairs)
            new_saved = matrix_product(group_reach, got_saved) + group_saved
        group_saved = new_saved
        step *= 2
    incoming = lax.ppermute(group_saved, "z", [(i, i + 1) for i in range(major - 1)])

    entry_reach = shift_down(reach, 1, identity)
    entry_saved = shift_down(saved, 1, 0.0)
    entry_state = matrix_product(entry_reach, incoming[None]) + entry_saved
    core_out = (
        jnp.einsum("bhcd,bhde->bhce", query_state, entry_state, precision=precise) + local_out
    )
    core_tokens = core_out.transpose(0, 2, 1, 3).reshape(tok_rows, local_heads, value_width)
    normed = gated_norm(
        core_tokens, gate_here.reshape(tok_rows, local_heads, value_width), norm_gain
    )
    normed = normed.reshape(tok_rows, local_heads * value_width)
    if GATHER_AS_A2A:
        copies = jnp.broadcast_to(normed[None], (minor,) + normed.shape)
        normed = lax.all_to_all(copies, "x", 0, 0, tiled=True)
        normed = normed.transpose(1, 0, 2).reshape(tok_rows, -1)
    else:
        normed = lax.all_gather(normed, "x", axis=1, tiled=True)
    groups = lax.psum(1, "heads")
    weight_rows = lax.all_gather(out_weight, "z", axis=1, tiled=True)
    partial_value = jnp.dot(normed, weight_rows, preferred_element_type=jnp.float32)
    partial_value = partial_value.astype(jnp.bfloat16)
    rows = tok_rows // minor
    pieces = partial_value.reshape(minor, rows, groups, major // groups, -1)
    if JOINT_A2A:
        pieces = pieces.transpose(0, 2, 1, 3, 4).reshape(minor * groups, rows, major // groups, -1)
        pieces = lax.all_to_all(pieces, ("x", "heads"), 0, 0, tiled=True)
        pieces = pieces.reshape(minor, groups, rows, major // groups, -1)
        summed = jnp.sum(pieces.astype(jnp.float32), axis=1).astype(jnp.bfloat16)
    else:
        pieces = lax.all_to_all(pieces, "heads", 2, 2, tiled=True)
        summed = jnp.sum(pieces.astype(jnp.float32), axis=2).astype(jnp.bfloat16)
        summed = lax.all_to_all(summed, "x", 0, 0, tiled=True)
    return summed.transpose(1, 2, 0, 3).reshape(rows, -1)


def solution(mesh):
    heads_size, seq_size = mesh.devices.shape
    minor = SEQ_MINOR
    major = seq_size // minor
    split_mesh = Mesh(mesh.devices.reshape(heads_size, major, minor), ("heads", "z", "x"))
    seq = ("z", "x")
    placed = (
        P(seq, "heads"),
        P(seq, "heads"),
        P(seq, "heads"),
        P(seq, "heads"),
        P("heads", seq),
        P("heads", seq),
        P(seq),
        P(),
        P("heads", seq),
    )

    def body(*arrays):
        return on_device(*arrays, minor=minor, major=major)

    return jax.shard_map(
        body, mesh=split_mesh, in_specs=placed, out_specs=P(seq, "heads"), check_vma=False
    )
```
